256 devices in a mesh: gx: 4 (over z_lo), gy: 8 (over z_hi, y), gz: 8 (over x, core).
Axes of the slice: x: 4, y: 4, z: 8 (z_hi: 2, z_lo: 4; z = z_hi * 4 + z_lo), core: 2. Of those that a mesh axis runs over, the one named last changes fastest.
Arguments:
- vectors: float32 [4, 5, 125, 4, 8, 1024], P(None, None, None, 'gx', 'gy', 'gz'), may hold values from -6 to 6
- stiffness: float32 [5, 5], replicated, may hold values from -2.5 to 2.5
- flux: float32 [3, 5, 5], replicated, may hold values from -1.25 to 1.25
- penalty: float32 [3, 5], replicated, may hold values from 0.2 to 2
- local_factor: float32 [5, 5], replicated, may hold values from -2.5 to 2.5
- element_field_factor: float32 [5, 5], replicated, may hold values from -2.5 to 2.5
- aggregate: int32 [4, 8, 1024], P('gx', 'gy', 'gz'), may hold values from 0 to 1023
- coarse_inverse: float32 [20480, 5120], P(('gx', 'gy', 'gz')), may hold values from -0.078125 to 0.078125
Outputs:
- result: float32 [4, 5, 125, 4, 8, 1024], P(None, None, None, 'gx', 'gy', 'gz')
The draws below stay inside these ranges and needn't reach their ends.
Inputs may be any that keep to these rules, and one draw needn't show every extreme that they name: aggregate numbers are counted within the elements of one index of gx.
All inputs are finite; a program needn't handle non-finite values.
Results may differ from the reference program's by a relative error of at most 0.0001.
Values sent between devices are 32-bit elements; how exact they have to be, the bound alone decides.
No kernel may reach another device: no remote copies, remote signals or barrier semaphores. Data moves between devices by JAX's collectives and lax.ppermute only.
A program may use at most 256 MiB of HBM per device.

```python
import math
import jax
import jax.numpy as jnp
from jax import lax

FIELD_COUNT = 5
VECTOR_COUNT = 4
EX = 1
ELEMENTS_FIRST = 4
ELEMENTS_SECOND = 8
ELEMENTS_THIRD = 1024
GROUP_AGGREGATES = 1024
CN = 5120
N_GX = 4


def place_ends(entries, rng, low, top_value):
    longest = entries.shape.index(max(entries.shape))
    spots = []
    for shift in (0, 1):
        where = [jax.random.randint(jax.random.fold_in(rng, axis), (), 0, length) for axis, length in enumerate(entries.shape)]
        where[longest] = (where[longest] + shift) % entries.shape[longest]
        spots.append(tuple(where))
    return entries.at[spots[0]].set(low).at[spots[1]].set(top_value)


def shard_levels(own_key, extent, pieces, low, top_value):
    level = 1.0
    for position, blocks in pieces:
        draws = jax.random.uniform(jax.random.fold_in(jax.random.fold_in(own_key, 6), position), (blocks,), jnp.float32, low / len(pieces), top_value / len(pieces))
        level = level * jnp.repeat(jnp.exp(draws), extent[position] // blocks).reshape((-1,) + (1,) * (len(extent) - 1 - position))
    return level


def scatter_about(stream_key, extent, deviation, reach, cuts=(), held_as=jnp.bfloat16):
    factor_of = shard_levels(stream_key, extent, cuts, -0.22, 0.18) if cuts else 1.0
    drawn = jax.random.normal(stream_key, extent, jnp.float32) * deviation * factor_of
    return jnp.minimum(jnp.maximum(drawn, -reach), reach).astype(held_as)


def setup_inputs(seed: int = 0) -> dict:
    keys = jax.random.split(jax.random.key(seed), 9)
    return {
        "vectors": scatter_about(keys[0], (VECTOR_COUNT, FIELD_COUNT, 125, ELEMENTS_FIRST, ELEMENTS_SECOND, ELEMENTS_THIRD), 1.0, 6.0, ((3, 4), (4, 8), (5, 8)), jnp.float32),
        "stiffness": scatter_about(keys[1], (5, 5), 5 ** -0.5, 2.5, (), jnp.float32),
        "flux": scatter_about(keys[2], (3, 5, 5), 20 ** -0.5, 1.25, (), jnp.float32),
        "penalty": jnp.clip(jnp.exp(jax.random.uniform(keys[3], (3, 5), jnp.float32, math.log(0.2), math.log(2.0))), 0.2, 2.0),
        "local_factor": scatter_about(keys[4], (5, 5), 5 ** -0.5, 2.5, (), jnp.float32),
        "element_field_factor": scatter_about(keys[5], (5, 5), 5 ** -0.5, 2.5, (), jnp.float32),
        "aggregate": place_ends(jax.random.randint(keys[6], (ELEMENTS_FIRST, ELEMENTS_SECOND, ELEMENTS_THIRD), 0, GROUP_AGGREGATES), jax.random.fold_in(keys[6], 1), 0, GROUP_AGGREGATES - 1).astype(jnp.int32),
        "coarse_inverse": scatter_about(keys[7], (N_GX * CN, CN), CN ** -0.5, 0.078125, ((0, 256),), jnp.float32),
    }


HIGH = lax.Precision.HIGHEST


def kron_three(first, second, third):
    return jnp.kron(jnp.kron(first, second), third)


def operator_matrix(stiffness, flux):
    unit = jnp.eye(5, dtype=jnp.float32)
    sweeps = [kron_three(stiffness, unit, unit), kron_three(unit, stiffness, unit), kron_three(unit, unit, stiffness)]
    total = jnp.zeros((625, 625), jnp.float32)
    for axis in range(3):
        total = total + jnp.kron(flux[axis], sweeps[axis])
    return total.reshape(5, 125, 5, 125)


def next_along(block, axis):
    count = block.shape[axis]
    widths = [(0, 0)] * block.ndim
    widths[axis] = (0, 1)
    return lax.slice_in_dim(jnp.pad(block, widths), 1, count + 1, axis=axis)


def prev_along(block, axis):
    count = block.shape[axis]
    widths = [(0, 0)] * block.ndim
    widths[axis] = (1, 0)
    return lax.slice_in_dim(jnp.pad(block, widths), 0, count, axis=axis)


def operate(field, big, penalty):
    output = field + jnp.einsum('fqgp,kgpxyz->kfqxyz', big, field, precision=HIGH)
    cube = field.reshape(field.shape[:2] + (5, 5, 5) + field.shape[3:])
    result = output.reshape(cube.shape)
    for axis in range(3):
        minus = jnp.take(cube, 0, axis=2 + axis)
        plus = jnp.take(cube, 4, axis=2 + axis)
        tau = penalty[axis][None, :, None, None, None, None, None]
        lead = (slice(None),) * (2 + axis)
        result = result.at[lead + (4,)].add(tau * (plus - next_along(minus, 4 + axis)))
        result = result.at[lead + (0,)].add(tau * (minus - prev_along(plus, 4 + axis)))
    return result.reshape(field.shape)


def precondition(field, local_kron, element_field_factor, aggregate, coarse_inverse):
    fine = jnp.einsum('qp,kfpxyz->kfqxyz', local_kron, field, precision=HIGH)
    fine = jnp.einsum('fg,kgqxyz->kfqxyz', element_field_factor, fine, precision=HIGH)
    means = jnp.sum(field, axis=2) * (1.0 / 125.0)
    nagg = coarse_inverse.shape[1] // FIELD_COUNT
    slabs = []
    for group in range(N_GX):
        ids = aggregate[group * EX:(group + 1) * EX].reshape(-1)
        block = means[:, :, group * EX:(group + 1) * EX].reshape(VECTOR_COUNT * FIELD_COUNT, -1)
        restricted = jax.ops.segment_sum(block.T, ids, num_segments=nagg).T
        flat = restricted.reshape(VECTOR_COUNT, FIELD_COUNT * nagg)
        rows = coarse_inverse[group * FIELD_COUNT * nagg:(group + 1) * FIELD_COUNT * nagg]
        coarse = jnp.einsum('kc,rc->kr', flat, rows, precision=HIGH)
        values = coarse.reshape(VECTOR_COUNT * FIELD_COUNT, nagg)[:, ids]
        slabs.append(values.reshape(VECTOR_COUNT, FIELD_COUNT, EX, means.shape[3], means.shape[4]))
    back = jnp.concatenate(slabs, axis=2)
    return fine + back[:, :, None, :, :, :]


def reference(vectors, stiffness, flux, penalty, local_factor, element_field_factor, aggregate, coarse_inverse):
    big = operator_matrix(stiffness, flux)
    local_kron = kron_three(local_factor, local_factor, local_factor)
    field = vectors
    for turn in range(2):
        field = precondition(field, local_kron, element_field_factor, aggregate, coarse_inverse)
        field = operate(field, big, penalty)
    return field
```

```python
import jax
import jax.numpy as jnp
import numpy as np
from jax import lax
from jax.sharding import PartitionSpec as P

HIGH = lax.Precision.HIGHEST


def neighbours(minus, plus, axis, dim):
    size, length = (lax.axis_size(axis), minus.shape[dim])
    up = [(i, i + 1) for i in range(size - 1)]
    down = [(i + 1, i) for i in range(size - 1)]
    last_plus = lax.slice_in_dim(plus, length - 1, length, axis=dim)
    first_minus = lax.slice_in_dim(minus, 0, 1, axis=dim)
    from_prev = lax.ppermute(last_plus, axis, up)
    from_next = lax.ppermute(first_minus, axis, down)
    before = jnp.concatenate([from_prev, lax.slice_in_dim(plus, 0, length - 1, axis=dim)], axis=dim)
    after = jnp.concatenate([lax.slice_in_dim(minus, 1, length, axis=dim), from_next], axis=dim)
    return after, before


def swap(x, axis, k):
    size = lax.axis_size(axis)
    return lax.ppermute(x, axis, [(i, i ^ k) for i in range(size)])


def bits_of(axes):
    order = []
    for axis in axes:
        size = lax.axis_size(axis)
        k = 1
        while k < size:
            order.append((axis, k))
            k *= 2
    return order


def is_pow2(n):
    return n > 0 and (n & (n - 1)) == 0


def group_sum(x, axes):
    order = bits_of(axes)
    width = x.shape[-1]
    if not all(is_pow2(lax.axis_size(a)) for a in axes) or width % (1 << len(order)):
        return lax.psum(x, axes)
    for axis, k in order:
        bit = (lax.axis_index(axis) // k) % 2
        half = x.shape[-1] // 2
        low, high = x[..., :half], x[..., half:]
        send = jnp.where(bit == 0, high, low)
        keep = jnp.where(bit == 0, low, high)
        x = keep + swap(send, axis, k)
    for axis, k in reversed(order):
        bit = (lax.axis_index(axis) // k) % 2
        other = swap(x, axis, k)
        x = jnp.where(bit == 0, jnp.concatenate([x, other], -1), jnp.concatenate([other, x], -1))
    return x


def group_gather(y, axes):
    if not all(is_pow2(lax.axis_size(a)) for a in axes):
        return lax.all_gather(y, axes, axis=y.ndim - 1, tiled=True)
    width = y.shape[-1]
    for axis, k in bits_of(axes):
        bit = (lax.axis_index(axis) // k) % 2
        other = swap(y, axis, k)
        y = jnp.where(bit == 0, jnp.concatenate([y, other], -1), jnp.concatenate([other, y], -1))
    sizes = [lax.axis_size(a) for a in axes]
    lead = y.shape[:-1]
    y = y.reshape(lead + tuple(sizes[::-1]) + (width,))
    count = len(lead)
    perm = list(range(count)) + [count + len(axes) - 1 - i for i in range(len(axes))] + [count + len(axes)]
    y = jnp.transpose(y, perm)
    return y.reshape(lead + (-1,))


def kron_three(first, second, third):
    return jnp.kron(jnp.kron(first, second), third)


def operator_matrix(stiffness, flux):
    unit = jnp.eye(5, dtype=jnp.float32)
    sweeps = [
        kron_three(stiffness, unit, unit),
        kron_three(unit, stiffness, unit),
        kron_three(unit, unit, stiffness),
    ]
    total = jnp.zeros((625, 625), jnp.float32)
    for axis in range(3):
        total = total + jnp.kron(flux[axis], sweeps[axis])
    return total.reshape(5, 125, 5, 125)


def face_table():
    table = np.zeros((150, 125), np.float32)
    for axis in range(3):
        for side in range(2):
            level = 4 * side
            for first in range(5):
                for second in range(5):
                    if axis == 0:
                        node = 25 * level + 5 * first + second
                    elif axis == 1:
                        node = 25 * first + 5 * level + second
                    else:
                        node = 25 * first + 5 * second + level
                    table[50 * axis + 25 * side + 5 * first + second, node] = 1.0
    return table


def operate(flat, dims, big, penalty, selects):
    vecs, fields, elements = (flat.shape[0], flat.shape[1], flat.shape[3])
    output = flat + jnp.einsum("fqgp,kgpe->kfqe", big, flat, precision=HIGH)
    faces = jnp.einsum("sq,kfqe->kfse", selects, flat, precision=HIGH)
    shaped = (vecs, fields, 25) + dims
    pairs = []
    for axis in range(3):
        minus = faces[:, :, 50 * axis : 50 * axis + 25].reshape(shaped)
        plus = faces[:, :, 50 * axis + 25 : 50 * axis + 50].reshape(shaped)
        pairs.append((minus, plus))
    neighbours_of = []
    for axis, name in enumerate(("gx", "gy", "gz")):
        minus, plus = pairs[axis]
        neighbours_of.append(neighbours(minus, plus, name, 3 + axis))
    terms = []
    for axis in range(3):
        minus, plus = pairs[axis]
        tau = penalty[axis][None, :, None, None, None, None]
        terms.append((tau * (minus - neighbours_of[axis][1])).reshape(vecs, fields, 25, elements))
        terms.append((tau * (plus - neighbours_of[axis][0])).reshape(vecs, fields, 25, elements))
    stacked = jnp.concatenate(terms, axis=2)
    return output + jnp.einsum("sq,kfse->kfqe", selects, stacked, precision=HIGH)


def precondition(flat, local_kron, element_field_factor, onehot, coarse_inverse):
    vecs, fields, elements = (flat.shape[0], flat.shape[1], flat.shape[3])
    fine = jnp.einsum("qp,kfpe->kfqe", local_kron, flat, precision=HIGH)
    fine = jnp.einsum("fg,kgqe->kfqe", element_field_factor, fine, precision=HIGH)
    nagg = coarse_inverse.shape[1] // fields
    means = jnp.sum(flat, axis=2) * (1.0 / 125.0)
    block = means.reshape(vecs * fields, elements)
    partial_sum = jnp.dot(block, onehot, precision=HIGH)
    restricted = group_sum(partial_sum, ("gy", "gz"))
    merged = restricted.reshape(vecs, fields * nagg)
    owned = jnp.einsum("kc,rc->kr", merged, coarse_inverse, precision=HIGH)
    coarse = group_gather(owned, ("gy", "gz"))
    values = jnp.dot(coarse.reshape(vecs * fields, nagg), onehot.T, precision=HIGH)
    back = values.reshape(vecs, fields, elements)
    return fine + back[:, :, None, :]


def on_device(
    vectors, stiffness, flux, penalty, local_factor, element_field_factor, aggregate, coarse_inverse
):
    big = operator_matrix(stiffness, flux)
    local_kron = kron_three(local_factor, local_factor, local_factor)
    selects = jnp.asarray(face_table())
    dims = tuple(vectors.shape[3:])
    elements = aggregate.size
    nagg = coarse_inverse.shape[1] // vectors.shape[1]
    onehot = (
        aggregate.reshape(elements)[:, None] == jnp.arange(nagg, dtype=jnp.int32)[None, :]
    ).astype(jnp.float32)
    flat = vectors.reshape(vectors.shape[:3] + (elements,))
    for turn in range(2):
        flat = precondition(flat, local_kron, element_field_factor, onehot, coarse_inverse)
        flat = operate(flat, dims, big, penalty, selects)
    return flat.reshape(vectors.shape)


def solution(mesh):
    placed = (
        P(None, None, None, "gx", "gy", "gz"),
        P(),
        P(),
        P(),
        P(),
        P(),
        P("gx", "gy", "gz"),
        P(("gx", "gy", "gz"), None),
    )
    return jax.shard_map(
        on_device,
        mesh=mesh,
        in_specs=placed,
        out_specs=P(None, None, None, "gx", "gy", "gz"),
        check_vma=False,
    )
```

```python
import jax
import jax.numpy as jnp
import numpy as np
from jax import lax
from jax.sharding import PartitionSpec as P

HIGH = lax.Precision.HIGHEST


def neighbours(minus, plus, axis, dim):
    size, length = (lax.axis_size(axis), minus.shape[dim])
    up = [(i, i + 1) for i in range(size - 1)]
    down = [(i + 1, i) for i in range(size - 1)]
    last_plus = lax.slice_in_dim(plus, length - 1, length, axis=dim)
    first_minus = lax.slice_in_dim(minus, 0, 1, axis=dim)
    from_prev = lax.ppermute(last_plus, axis, up)
    from_next = lax.ppermute(first_minus, axis, down)
    before = jnp.concatenate([from_prev, lax.slice_in_dim(plus, 0, length - 1, axis=dim)], axis=dim)
    after = jnp.concatenate([lax.slice_in_dim(minus, 1, length, axis=dim), from_next], axis=dim)
    return after, before


def swap(x, axis, k):
    size = lax.axis_size(axis)
    return lax.ppermute(x, axis, [(i, i ^ k) for i in range(size)])


def bits_of(axes):
    order = []
    for axis in axes:
        size = lax.axis_size(axis)
        k = 1
        while k < size:
            order.append((axis, k))
            k *= 2
    return order


def is_pow2(n):
    return n > 0 and (n & (n - 1)) == 0


def group_sum(x, axes):
    order = bits_of(axes)
    width = x.shape[-1]
    if not all(is_pow2(lax.axis_size(a)) for a in axes) or width % (1 << len(order)):
        return lax.psum(x, axes)
    for axis, k in order:
        bit = (lax.axis_index(axis) // k) % 2
        half = x.shape[-1] // 2
        low, high = x[..., :half], x[..., half:]
        send = jnp.where(bit == 0, high, low)
        keep = jnp.where(bit == 0, low, high)
        x = keep + swap(send, axis, k)
    for axis, k in reversed(order):
        bit = (lax.axis_index(axis) // k) % 2
        other = swap(x, axis, k)
        x = jnp.where(bit == 0, jnp.concatenate([x, other], -1), jnp.concatenate([other, x], -1))
    return x


def group_gather(y, axes):
    if not all(is_pow2(lax.axis_size(a)) for a in axes):
        return lax.all_gather(y, axes, axis=y.ndim - 1, tiled=True)
    width = y.shape[-1]
    for axis, k in bits_of(axes):
        bit = (lax.axis_index(axis) // k) % 2
        other = swap(y, axis, k)
        y = jnp.where(bit == 0, jnp.concatenate([y, other], -1), jnp.concatenate([other, y], -1))
    sizes = [lax.axis_size(a) for a in axes]
    lead = y.shape[:-1]
    y = y.reshape(lead + tuple(sizes[::-1]) + (width,))
    count = len(lead)
    perm = list(range(count)) + [count + len(axes) - 1 - i for i in range(len(axes))] + [count + len(axes)]
    y = jnp.transpose(y, perm)
    return y.reshape(lead + (-1,))


def kron_three(first, second, third):
    return jnp.kron(jnp.kron(first, second), third)


def operator_matrix(stiffness, flux):
    unit = jnp.eye(5, dtype=jnp.float32)
    sweeps = [
        kron_three(stiffness, unit, unit),
        kron_three(unit, stiffness, unit),
        kron_three(unit, unit, stiffness),
    ]
    total = jnp.zeros((625, 625), jnp.float32)
    for axis in range(3):
        total = total + jnp.kron(flux[axis], sweeps[axis])
    return total.reshape(5, 125, 5, 125)


def face_table():
    table = np.zeros((150, 125), np.float32)
    for axis in range(3):
        for side in range(2):
            level = 4 * side
            for first in range(5):
                for second in range(5):
                    if axis == 0:
                        node = 25 * level + 5 * first + second
                    elif axis == 1:
                        node = 25 * first + 5 * level + second
                    else:
                        node = 25 * first + 5 * second + level
                    table[50 * axis + 25 * side + 5 * first + second, node] = 1.0
    return table


def operate(flat, dims, big, penalty, selects):
    vecs, fields, elements = (flat.shape[0], flat.shape[1], flat.shape[3])
    output = flat + jnp.einsum("fqgp,kgpe->kfqe", big, flat, precision=HIGH)
    faces = jnp.einsum("sq,kfqe->kfse", selects, flat, precision=HIGH)
    shaped = (vecs, fields, 25) + dims
    pairs = []
    for axis in range(3):
        minus = faces[:, :, 50 * axis : 50 * axis + 25].reshape(shaped)
        plus = faces[:, :, 50 * axis + 25 : 50 * axis + 50].reshape(shaped)
        pairs.append((minus, plus))
    neighbours_of = []
    for axis, name in enumerate(("gx", "gy", "gz")):
        minus, plus = pairs[axis]
        neighbours_of.append(neighbours(minus, plus, name, 3 + axis))
    terms = []
    for axis in range(3):
        minus, plus = pairs[axis]
        tau = penalty[axis][None, :, None, None, None, None]
        terms.append((tau * (minus - neighbours_of[axis][1])).reshape(vecs, fields, 25, elements))
        terms.append((tau * (plus - neighbours_of[axis][0])).reshape(vecs, fields, 25, elements))
    stacked = jnp.concatenate(terms, axis=2)
    return output + jnp.einsum("sq,kfse->kfqe", selects, stacked, precision=HIGH)


def fine_part(flat, local_kron, element_field_factor):
    fine = jnp.einsum("qp,kfpe->kfqe", local_kron, flat, precision=HIGH)
    return jnp.einsum("fg,kgqe->kfqe", element_field_factor, fine, precision=HIGH)


def coarse_part(means, onehot, coarse_inverse):
    vecs, fields, elements = means.shape
    nagg = coarse_inverse.shape[1] // fields
    block = means.reshape(vecs * fields, elements)
    partial_sum = jnp.dot(block, onehot, precision=HIGH)
    restricted = group_sum(partial_sum, ("gy", "gz"))
    merged = restricted.reshape(vecs, fields * nagg)
    owned = jnp.einsum("kc,rc->kr", merged, coarse_inverse, precision=HIGH)
    coarse = group_gather(owned, ("gy", "gz"))
    values = jnp.dot(coarse.reshape(vecs * fields, nagg), onehot.T, precision=HIGH)
    return values.reshape(vecs, fields, elements)


def constant_table(stiffness):
    rows = jnp.sum(stiffness, axis=1)
    node = np.arange(125)
    index = [node // 25, (node // 5) % 5, node % 5]
    columns = [jnp.ones((125,), jnp.float32)]
    columns += [rows[index[d]] for d in range(3)]
    columns += [jnp.asarray((index[d] == 4).astype(np.float32)) for d in range(3)]
    columns += [jnp.asarray((index[d] == 0).astype(np.float32)) for d in range(3)]
    return jnp.stack(columns, axis=1)


def constant_terms(back, dims, flux, penalty):
    vecs, fields, elements = back.shape
    cube = back.reshape((vecs, fields) + dims)
    terms = [back]
    terms += [jnp.einsum("fg,kge->kfe", flux[d], back, precision=HIGH) for d in range(3)]
    ahead, behind = [], []
    for d, name in enumerate(("gx", "gy", "gz")):
        after, before = neighbours(cube, cube, name, 2 + d)
        tau = penalty[d][None, :, None]
        ahead.append(tau * (back - after.reshape(vecs, fields, elements)))
        behind.append(tau * (back - before.reshape(vecs, fields, elements)))
    return jnp.stack(terms + ahead + behind, axis=2)


def on_device(
    vectors, stiffness, flux, penalty, local_factor, element_field_factor, aggregate, coarse_inverse
):
    big = operator_matrix(stiffness, flux)
    local_kron = kron_three(local_factor, local_factor, local_factor)
    selects = jnp.asarray(face_table())
    table = constant_table(stiffness)
    table_mean = jnp.sum(table, axis=0) * (1.0 / 125.0)
    dims = tuple(vectors.shape[3:])
    elements = aggregate.size
    nagg = coarse_inverse.shape[1] // vectors.shape[1]
    onehot = (
        aggregate.reshape(elements)[:, None] == jnp.arange(nagg, dtype=jnp.int32)[None, :]
    ).astype(jnp.float32)
    flat = vectors.reshape(vectors.shape[:3] + (elements,))
    means = jnp.sum(flat, axis=2) * (1.0 / 125.0)
    for turn in range(2):
        applied = operate(fine_part(flat, local_kron, element_field_factor), dims, big, penalty, selects)
        back = coarse_part(means, onehot, coarse_inverse)
        stacked = constant_terms(back, dims, flux, penalty)
        flat = applied + jnp.einsum("qt,kfte->kfqe", table, stacked, precision=HIGH)
        if turn == 0:
            means = jnp.sum(applied, axis=2) * (1.0 / 125.0) + jnp.einsum(
                "t,kfte->kfe", table_mean, stacked, precision=HIGH
            )
    return flat.reshape(vectors.shape)


def solution(mesh):
    placed = (
        P(None, None, None, "gx", "gy", "gz"),
        P(),
        P(),
        P(),
        P(),
        P(),
        P("gx", "gy", "gz"),
        P(("gx", "gy", "gz"), None),
    )
    return jax.shard_map(
        on_device,
        mesh=mesh,
        in_specs=placed,
        out_specs=P(None, None, None, "gx", "gy", "gz"),
        check_vma=False,
    )
```

```python
import jax
import jax.numpy as jnp
import numpy as np
from jax import lax
from jax.sharding import PartitionSpec as P

HIGH = lax.Precision.HIGHEST


def neighbours(minus, plus, axis, dim):
    size, length = (lax.axis_size(axis), minus.shape[dim])
    up = [(i, i + 1) for i in range(size - 1)]
    down = [(i + 1, i) for i in range(size - 1)]
    last_plus = lax.slice_in_dim(plus, length - 1, length, axis=dim)
    first_minus = lax.slice_in_dim(minus, 0, 1, axis=dim)
    from_prev = lax.ppermute(last_plus, axis, up)
    from_next = lax.ppermute(first_minus, axis, down)
    before = jnp.concatenate([from_prev, lax.slice_in_dim(plus, 0, length - 1, axis=dim)], axis=dim)
    after = jnp.concatenate([lax.slice_in_dim(minus, 1, length, axis=dim), from_next], axis=dim)
    return after, before


def swap(x, axis, k):
    size = lax.axis_size(axis)
    return lax.ppermute(x, axis, [(i, i ^ k) for i in range(size)])


def bits_of(axes):
    order = []
    for axis in axes:
        size = lax.axis_size(axis)
        k = 1
        while k < size:
            order.append((axis, k))
            k *= 2
    return order


def is_pow2(n):
    return n > 0 and (n & (n - 1)) == 0


def group_sum(x, axes):
    order = bits_of(axes)
    width = x.shape[-1]
    if not all(is_pow2(lax.axis_size(a)) for a in axes) or width % (1 << len(order)):
        return lax.psum(x, axes)
    for axis, k in order:
        bit = (lax.axis_index(axis) // k) % 2
        half = x.shape[-1] // 2
        low, high = x[..., :half], x[..., half:]
        send = jnp.where(bit == 0, high, low)
        keep = jnp.where(bit == 0, low, high)
        x = keep + swap(send, axis, k)
    for axis, k in reversed(order):
        bit = (lax.axis_index(axis) // k) % 2
        other = swap(x, axis, k)
        x = jnp.where(bit == 0, jnp.concatenate([x, other], -1), jnp.concatenate([other, x], -1))
    return x


def group_gather(y, axes):
    if not all(is_pow2(lax.axis_size(a)) for a in axes):
        return lax.all_gather(y, axes, axis=y.ndim - 1, tiled=True)
    width = y.shape[-1]
    for axis, k in bits_of(axes):
        bit = (lax.axis_index(axis) // k) % 2
        other = swap(y, axis, k)
        y = jnp.where(bit == 0, jnp.concatenate([y, other], -1), jnp.concatenate([other, y], -1))
    sizes = [lax.axis_size(a) for a in axes]
    lead = y.shape[:-1]
    y = y.reshape(lead + tuple(sizes[::-1]) + (width,))
    count = len(lead)
    perm = list(range(count)) + [count + len(axes) - 1 - i for i in range(len(axes))] + [count + len(axes)]
    y = jnp.transpose(y, perm)
    return y.reshape(lead + (-1,))


def node_index():
    node = np.arange(125)
    return [node // 25, (node // 5) % 5, node % 5]


def spread(matrix, d):
    picks = jnp.asarray((node_index()[d][:, None] == np.arange(5)[None, :]).astype(np.float32))
    return jnp.dot(jnp.dot(picks, matrix, precision=HIGH), picks.T, precision=HIGH)


def same_except(d):
    index = node_index()
    keep = np.ones((125, 125), bool)
    for other in range(3):
        if other != d:
            keep &= index[other][:, None] == index[other][None, :]
    return jnp.asarray(keep.astype(np.float32))


def operator_matrix(stiffness, flux):
    total = 0.0
    for d in range(3):
        sweep = spread(stiffness, d) * same_except(d)
        total = total + flux[d][:, None, :, None] * sweep[None, :, None, :]
    return total


def fine_matrix(local_factor, element_field_factor):
    local = spread(local_factor, 0) * spread(local_factor, 1) * spread(local_factor, 2)
    return element_field_factor[:, None, :, None] * local[None, :, None, :]


def operate(flat, dims, big, penalty):
    vecs, fields, elements = (flat.shape[0], flat.shape[1], flat.shape[3])
    output = flat + jnp.einsum("fqgp,kgpe->kfqe", big, flat, precision=HIGH)
    cube = flat.reshape((vecs, fields, 5, 5, 5, elements))
    shaped = (vecs, fields, 25) + dims
    result = output.reshape(cube.shape)
    for d, name in enumerate(("gx", "gy", "gz")):
        minus = lax.index_in_dim(cube, 0, axis=2 + d, keepdims=False).reshape(shaped)
        plus = lax.index_in_dim(cube, 4, axis=2 + d, keepdims=False).reshape(shaped)
        after, before = neighbours(minus, plus, name, 3 + d)
        tau = penalty[d][None, :, None, None, None, None]
        low = (tau * (minus - before)).reshape((vecs, fields, 5, 5, elements))
        high = (tau * (plus - after)).reshape((vecs, fields, 5, 5, elements))
        widths = [(0, 0)] * 6
        widths[2 + d] = (0, 4)
        result = result + jnp.pad(jnp.expand_dims(low, 2 + d), widths)
        widths[2 + d] = (4, 0)
        result = result + jnp.pad(jnp.expand_dims(high, 2 + d), widths)
    return result.reshape(flat.shape)


def precondition(flat, fine_op, onehot, coarse_inverse):
    vecs, fields, elements = (flat.shape[0], flat.shape[1], flat.shape[3])
    fine = jnp.einsum("fqgp,kgpe->kfqe", fine_op, flat, precision=HIGH)
    nagg = coarse_inverse.shape[1] // fields
    means = jnp.sum(flat, axis=2) * (1.0 / 125.0)
    block = means.reshape(vecs * fields, elements)
    partial_sum = jnp.dot(block, onehot, precision=HIGH)
    restricted = group_sum(partial_sum, ("gy", "gz"))
    merged = restricted.reshape(vecs, fields * nagg)
    owned = jnp.einsum("kc,rc->kr", merged, coarse_inverse, precision=HIGH)
    coarse = group_gather(owned, ("gy", "gz"))
    values = jnp.dot(coarse.reshape(vecs * fields, nagg), onehot.T, precision=HIGH)
    back = values.reshape(vecs, fields, elements)
    return fine + back[:, :, None, :]


def on_device(
    vectors, stiffness, flux, penalty, local_factor, element_field_factor, aggregate, coarse_inverse
):
    big = operator_matrix(stiffness, flux)
    fine_op = fine_matrix(local_factor, element_field_factor)
    dims = tuple(vectors.shape[3:])
    elements = aggregate.size
    nagg = coarse_inverse.shape[1] // vectors.shape[1]
    onehot = (
        aggregate.reshape(elements)[:, None] == jnp.arange(nagg, dtype=jnp.int32)[None, :]
    ).astype(jnp.float32)
    flat = vectors.reshape(vectors.shape[:3] + (elements,))
    for turn in range(2):
        flat = precondition(flat, fine_op, onehot, coarse_inverse)
        flat = operate(flat, dims, big, penalty)
    return flat.reshape(vectors.shape)


def solution(mesh):
    placed = (
        P(None, None, None, "gx", "gy", "gz"),
        P(),
        P(),
        P(),
        P(),
        P(),
        P("gx", "gy", "gz"),
        P(("gx", "gy", "gz"), None),
    )
    return jax.shard_map(
        on_device,
        mesh=mesh,
        in_specs=placed,
        out_specs=P(None, None, None, "gx", "gy", "gz"),
        check_vma=False,
    )
```

```python
import jax
import jax.numpy as jnp
import numpy as np
from jax import lax
from jax.sharding import PartitionSpec as P

HIGH = lax.Precision.HIGHEST


def neighbours(minus, plus, axis, dim):
    size, length = (lax.axis_size(axis), minus.shape[dim])
    up = [(i, i + 1) for i in range(size - 1)]
    down = [(i + 1, i) for i in range(size - 1)]
    last_plus = lax.slice_in_dim(plus, length - 1, length, axis=dim)
    first_minus = lax.slice_in_dim(minus, 0, 1, axis=dim)
    from_prev = lax.ppermute(last_plus, axis, up)
    from_next = lax.ppermute(first_minus, axis, down)
    before = jnp.concatenate([from_prev, lax.slice_in_dim(plus, 0, length - 1, axis=dim)], axis=dim)
    after = jnp.concatenate([lax.slice_in_dim(minus, 1, length, axis=dim), from_next], axis=dim)
    return after, before


def swap(x, axis, k):
    size = lax.axis_size(axis)
    return lax.ppermute(x, axis, [(i, i ^ k) for i in range(size)])


def bits_of(axes):
    order = []
    for axis in axes:
        size = lax.axis_size(axis)
        k = 1
        while k < size:
            order.append((axis, k))
            k *= 2
    return order


def is_pow2(n):
    return n > 0 and (n & (n - 1)) == 0


def group_sum(x, halved, exchanged):
    order = bits_of(halved)
    axes = tuple(halved) + tuple(exchanged)
    width = x.shape[-1]
    if not all(is_pow2(lax.axis_size(a)) for a in axes) or width % (1 << len(order)):
        return lax.psum(x, axes)
    for axis, k in order:
        bit = (lax.axis_index(axis) // k) % 2
        half = x.shape[-1] // 2
        low, high = x[..., :half], x[..., half:]
        send = jnp.where(bit == 0, high, low)
        keep = jnp.where(bit == 0, low, high)
        x = keep + swap(send, axis, k)
    for axis, k in bits_of(exchanged):
        x = x + swap(x, axis, k)
    for axis, k in reversed(order):
        bit = (lax.axis_index(axis) // k) % 2
        other = swap(x, axis, k)
        x = jnp.where(bit == 0, jnp.concatenate([x, other], -1), jnp.concatenate([other, x], -1))
    return x


def group_gather(y, axes):
    if not all(is_pow2(lax.axis_size(a)) for a in axes):
        return lax.all_gather(y, axes, axis=y.ndim - 1, tiled=True)
    width = y.shape[-1]
    for axis, k in bits_of(axes):
        bit = (lax.axis_index(axis) // k) % 2
        other = swap(y, axis, k)
        y = jnp.where(bit == 0, jnp.concatenate([y, other], -1), jnp.concatenate([other, y], -1))
    sizes = [lax.axis_size(a) for a in axes]
    lead = y.shape[:-1]
    y = y.reshape(lead + tuple(sizes[::-1]) + (width,))
    count = len(lead)
    perm = list(range(count)) + [count + len(axes) - 1 - i for i in range(len(axes))] + [count + len(axes)]
    y = jnp.transpose(y, perm)
    return y.reshape(lead + (-1,))


def node_index():
    node = np.arange(125)
    return [node // 25, (node // 5) % 5, node % 5]


def spread(matrix, d):
    picks = jnp.asarray((node_index()[d][:, None] == np.arange(5)[None, :]).astype(np.float32))
    return jnp.dot(jnp.dot(picks, matrix, precision=HIGH), picks.T, precision=HIGH)


def same_except(d):
    index = node_index()
    keep = np.ones((125, 125), bool)
    for other in range(3):
        if other != d:
            keep &= index[other][:, None] == index[other][None, :]
    return jnp.asarray(keep.astype(np.float32))


def operator_matrix(stiffness, flux):
    total = 0.0
    for d in range(3):
        sweep = spread(stiffness, d) * same_except(d)
        total = total + flux[d][:, None, :, None] * sweep[None, :, None, :]
    return total


def fine_matrix(local_factor, element_field_factor):
    local = spread(local_factor, 0) * spread(local_factor, 1) * spread(local_factor, 2)
    return element_field_factor[:, None, :, None] * local[None, :, None, :]


def operate(flat, dims, big, penalty):
    vecs, fields, elements = (flat.shape[0], flat.shape[1], flat.shape[3])
    output = flat + jnp.einsum("fqgp,kgpe->kfqe", big, flat, precision=HIGH)
    cube = flat.reshape((vecs, fields, 5, 5, 5, elements))
    shaped = (vecs, fields, 25) + dims
    result = output.reshape(cube.shape)
    for d, name in enumerate(("gx", "gy", "gz")):
        minus = lax.index_in_dim(cube, 0, axis=2 + d, keepdims=False).reshape(shaped)
        plus = lax.index_in_dim(cube, 4, axis=2 + d, keepdims=False).reshape(shaped)
        after, before = neighbours(minus, plus, name, 3 + d)
        tau = penalty[d][None, :, None, None, None, None]
        low = (tau * (minus - before)).reshape((vecs, fields, 5, 5, elements))
        high = (tau * (plus - after)).reshape((vecs, fields, 5, 5, elements))
        widths = [(0, 0)] * 6
        widths[2 + d] = (0, 4)
        result = result + jnp.pad(jnp.expand_dims(low, 2 + d), widths)
        widths[2 + d] = (4, 0)
        result = result + jnp.pad(jnp.expand_dims(high, 2 + d), widths)
    return result.reshape(flat.shape)


def precondition(flat, fine_op, onehot, coarse_inverse):
    vecs, fields, elements = (flat.shape[0], flat.shape[1], flat.shape[3])
    fine = jnp.einsum("fqgp,kgpe->kfqe", fine_op, flat, precision=HIGH)
    nagg = coarse_inverse.shape[1] // fields
    means = jnp.sum(flat, axis=2) * (1.0 / 125.0)
    block = means.reshape(vecs * fields, elements)
    partial_sum = jnp.dot(block, onehot, precision=HIGH)
    restricted = group_sum(partial_sum, ("gz",), ("gy",))
    merged = restricted.reshape(vecs, fields * nagg)
    owned = jnp.einsum("kc,rc->kr", merged, coarse_inverse, precision=HIGH)
    coarse = group_gather(owned, ("gy", "gz"))
    values = jnp.dot(coarse.reshape(vecs * fields, nagg), onehot.T, precision=HIGH)
    back = values.reshape(vecs, fields, elements)
    return fine + back[:, :, None, :]


def on_device(
    vectors, stiffness, flux, penalty, local_factor, element_field_factor, aggregate, coarse_inverse
):
    big = operator_matrix(stiffness, flux)
    fine_op = fine_matrix(local_factor, element_field_factor)
    dims = tuple(vectors.shape[3:])
    elements = aggregate.size
    nagg = coarse_inverse.shape[1] // vectors.shape[1]
    onehot = (
        aggregate.reshape(elements)[:, None] == jnp.arange(nagg, dtype=jnp.int32)[None, :]
    ).astype(jnp.float32)
    flat = vectors.reshape(vectors.shape[:3] + (elements,))
    for turn in range(2):
        flat = precondition(flat, fine_op, onehot, coarse_inverse)
        flat = operate(flat, dims, big, penalty)
    return flat.reshape(vectors.shape)


def solution(mesh):
    placed = (
        P(None, None, None, "gx", "gy", "gz"),
        P(),
        P(),
        P(),
        P(),
        P(),
        P("gx", "gy", "gz"),
        P(("gx", "gy", "gz"), None),
    )
    return jax.shard_map(
        on_device,
        mesh=mesh,
        in_specs=placed,
        out_specs=P(None, None, None, "gx", "gy", "gz"),
        check_vma=False,
    )
```

```python
import jax
import jax.numpy as jnp
import numpy as np
from jax import lax
from jax.sharding import PartitionSpec as P

HIGH = lax.Precision.HIGHEST


def neighbours(minus, plus, axis, dim):
    size, length = (lax.axis_size(axis), minus.shape[dim])
    up = [(i, i + 1) for i in range(size - 1)]
    down = [(i + 1, i) for i in range(size - 1)]
    last_plus = lax.slice_in_dim(plus, length - 1, length, axis=dim)
    first_minus = lax.slice_in_dim(minus, 0, 1, axis=dim)
    from_prev = lax.ppermute(last_plus, axis, up)
    from_next = lax.ppermute(first_minus, axis, down)
    before = jnp.concatenate([from_prev, lax.slice_in_dim(plus, 0, length - 1, axis=dim)], axis=dim)
    after = jnp.concatenate([lax.slice_in_dim(minus, 1, length, axis=dim), from_next], axis=dim)
    return after, before


def swap(x, axis, k):
    size = lax.axis_size(axis)
    return lax.ppermute(x, axis, [(i, i ^ k) for i in range(size)])


def bits_of(axes):
    order = []
    for axis in axes:
        size = lax.axis_size(axis)
        k = 1
        while k < size:
            order.append((axis, k))
            k *= 2
    return order


def is_pow2(n):
    return n > 0 and (n & (n - 1)) == 0


def group_sum(x, halved, exchanged):
    order = bits_of(halved)
    axes = tuple(halved) + tuple(exchanged)
    width = x.shape[-1]
    if not all(is_pow2(lax.axis_size(a)) for a in axes) or width % (1 << len(order)):
        return lax.psum(x, axes)
    for axis, k in order:
        bit = (lax.axis_index(axis) // k) % 2
        half = x.shape[-1] // 2
        low, high = x[..., :half], x[..., half:]
        send = jnp.where(bit == 0, high, low)
        keep = jnp.where(bit == 0, low, high)
        x = keep + swap(send, axis, k)
    for axis, k in bits_of(exchanged):
        x = x + swap(x, axis, k)
    for axis, k in reversed(order):
        bit = (lax.axis_index(axis) // k) % 2
        other = swap(x, axis, k)
        x = jnp.where(bit == 0, jnp.concatenate([x, other], -1), jnp.concatenate([other, x], -1))
    return x


def group_gather(y, axes):
    if not all(is_pow2(lax.axis_size(a)) for a in axes):
        return lax.all_gather(y, axes, axis=y.ndim - 1, tiled=True)
    width = y.shape[-1]
    for axis, k in bits_of(axes):
        bit = (lax.axis_index(axis) // k) % 2
        other = swap(y, axis, k)
        y = jnp.where(bit == 0, jnp.concatenate([y, other], -1), jnp.concatenate([other, y], -1))
    sizes = [lax.axis_size(a) for a in axes]
    lead = y.shape[:-1]
    y = y.reshape(lead + tuple(sizes[::-1]) + (width,))
    count = len(lead)
    perm = list(range(count)) + [count + len(axes) - 1 - i for i in range(len(axes))] + [count + len(axes)]
    y = jnp.transpose(y, perm)
    return y.reshape(lead + (-1,))


def node_index():
    node = np.arange(125)
    return [node // 25, (node // 5) % 5, node % 5]


def spread(matrix, d):
    picks = jnp.asarray((node_index()[d][:, None] == np.arange(5)[None, :]).astype(np.float32))
    return jnp.dot(jnp.dot(picks, matrix, precision=HIGH), picks.T, precision=HIGH)


def same_except(d):
    index = node_index()
    keep = np.ones((125, 125), bool)
    for other in range(3):
        if other != d:
            keep &= index[other][:, None] == index[other][None, :]
    return jnp.asarray(keep.astype(np.float32))


def operator_matrix(stiffness, flux):
    total = 0.0
    for d in range(3):
        sweep = spread(stiffness, d) * same_except(d)
        total = total + flux[d][:, None, :, None] * sweep[None, :, None, :]
    return total


def fine_matrix(local_factor, element_field_factor):
    local = spread(local_factor, 0) * spread(local_factor, 1) * spread(local_factor, 2)
    return element_field_factor[:, None, :, None] * local[None, :, None, :]


def operate(flat, dims, big, penalty):
    vecs, fields, elements = (flat.shape[0], flat.shape[1], flat.shape[3])
    output = flat + jnp.einsum("fqgp,kgpe->kfqe", big, flat, precision=HIGH)
    cube = flat.reshape((vecs, fields, 5, 5, 5, elements))
    shaped = (vecs, fields, 25) + dims
    result = output.reshape(cube.shape)
    for d, name in enumerate(("gx", "gy", "gz")):
        minus = lax.index_in_dim(cube, 0, axis=2 + d, keepdims=False).reshape(shaped)
        plus = lax.index_in_dim(cube, 4, axis=2 + d, keepdims=False).reshape(shaped)
        after, before = neighbours(minus, plus, name, 3 + d)
        tau = penalty[d][None, :, None, None, None, None]
        low = (tau * (minus - before)).reshape((vecs, fields, 5, 5, elements))
        high = (tau * (plus - after)).reshape((vecs, fields, 5, 5, elements))
        widths = [(0, 0)] * 6
        widths[2 + d] = (0, 4)
        result = result + jnp.pad(jnp.expand_dims(low, 2 + d), widths)
        widths[2 + d] = (4, 0)
        result = result + jnp.pad(jnp.expand_dims(high, 2 + d), widths)
    return result.reshape(flat.shape)


def precondition(flat, fine_op, onehot, coarse_inverse):
    vecs, fields, elements = (flat.shape[0], flat.shape[1], flat.shape[3])
    fine = jnp.einsum("fqgp,kgpe->kfqe", fine_op, flat, precision=HIGH)
    nagg = coarse_inverse.shape[1] // fields
    means = jnp.sum(flat, axis=2) * (1.0 / 125.0)
    block = means.reshape(vecs * fields, elements)
    partial_sum = jnp.dot(block, onehot, precision=HIGH)
    restricted = group_sum(partial_sum, ("gz",), ("gy",))
    merged = restricted.reshape(vecs, fields * nagg)
    owned = jnp.einsum("kc,rc->kr", merged, coarse_inverse, precision=HIGH)
    coarse = group_gather(owned, ("gy", "gz"))
    values = jnp.dot(coarse.reshape(vecs * fields, nagg), onehot.T, precision=HIGH)
    back = values.reshape(vecs, fields, elements)
    return fine + back[:, :, None, :]


def on_device(
    vectors, stiffness, flux, penalty, local_factor, element_field_factor, aggregate, coarse_inverse
):
    big = operator_matrix(stiffness, flux)
    fine_op = fine_matrix(local_factor, element_field_factor)
    dims = tuple(vectors.shape[3:])
    elements = aggregate.size
    nagg = coarse_inverse.shape[1] // vectors.shape[1]
    onehot = (
        aggregate.reshape(elements)[:, None] == jnp.arange(nagg, dtype=jnp.int32)[None, :]
    ).astype(jnp.float32)
    flat = vectors.reshape(vectors.shape[:3] + (elements,))
    def turn(_, flat):
        flat = precondition(flat, fine_op, onehot, coarse_inverse)
        return operate(flat, dims, big, penalty)

    flat = lax.fori_loop(0, 2, turn, flat)
    return flat.reshape(vectors.shape)


def solution(mesh):
    placed = (
        P(None, None, None, "gx", "gy", "gz"),
        P(),
        P(),
        P(),
        P(),
        P(),
        P("gx", "gy", "gz"),
        P(("gx", "gy", "gz"), None),
    )
    return jax.shard_map(
        on_device,
        mesh=mesh,
        in_specs=placed,
        out_specs=P(None, None, None, "gx", "gy", "gz"),
        check_vma=False,
    )
```

```python
import jax
import jax.numpy as jnp
import numpy as np
from jax import lax
from jax.sharding import PartitionSpec as P

HIGH = lax.Precision.HIGHEST


def neighbours(minus, plus, axis, dim):
    size, length = (lax.axis_size(axis), minus.shape[dim])
    up = [(i, i + 1) for i in range(size - 1)]
    down = [(i + 1, i) for i in range(size - 1)]
    last_plus = lax.slice_in_dim(plus, length - 1, length, axis=dim)
    first_minus = lax.slice_in_dim(minus, 0, 1, axis=dim)
    from_prev = lax.ppermute(last_plus, axis, up)
    from_next = lax.ppermute(first_minus, axis, down)
    before = jnp.concatenate([from_prev, lax.slice_in_dim(plus, 0, length - 1, axis=dim)], axis=dim)
    after = jnp.concatenate([lax.slice_in_dim(minus, 1, length, axis=dim), from_next], axis=dim)
    return after, before


def swap(x, axis, k):
    size = lax.axis_size(axis)
    return lax.ppermute(x, axis, [(i, i ^ k) for i in range(size)])


def bits_of(axes):
    order = []
    for axis in axes:
        size = lax.axis_size(axis)
        k = 1
        while k < size:
            order.append((axis, k))
            k *= 2
    return order


def is_pow2(n):
    return n > 0 and (n & (n - 1)) == 0


def group_sum(x, halved, exchanged):
    order = bits_of(halved)
    axes = tuple(halved) + tuple(exchanged)
    width = x.shape[-1]
    if not all(is_pow2(lax.axis_size(a)) for a in axes) or width % (1 << len(order)):
        return lax.psum(x, axes)
    for axis, k in order:
        bit = (lax.axis_index(axis) // k) % 2
        half = x.shape[-1] // 2
        low, high = x[..., :half], x[..., half:]
        send = jnp.where(bit == 0, high, low)
        keep = jnp.where(bit == 0, low, high)
        x = keep + swap(send, axis, k)
    for axis, k in bits_of(exchanged):
        x = x + swap(x, axis, k)
    for axis, k in reversed(order):
        bit = (lax.axis_index(axis) // k) % 2
        other = swap(x, axis, k)
        x = jnp.where(bit == 0, jnp.concatenate([x, other], -1), jnp.concatenate([other, x], -1))
    return x


def group_gather(y, axes):
    if not all(is_pow2(lax.axis_size(a)) for a in axes):
        return lax.all_gather(y, axes, axis=y.ndim - 1, tiled=True)
    width = y.shape[-1]
    for axis, k in bits_of(axes):
        bit = (lax.axis_index(axis) // k) % 2
        other = swap(y, axis, k)
        y = jnp.where(bit == 0, jnp.concatenate([y, other], -1), jnp.concatenate([other, y], -1))
    sizes = [lax.axis_size(a) for a in axes]
    lead = y.shape[:-1]
    y = y.reshape(lead + tuple(sizes[::-1]) + (width,))
    count = len(lead)
    perm = list(range(count)) + [count + len(axes) - 1 - i for i in range(len(axes))] + [count + len(axes)]
    y = jnp.transpose(y, perm)
    return y.reshape(lead + (-1,))


def node_index():
    node = np.arange(125)
    return [node // 25, (node // 5) % 5, node % 5]


def spread(matrix, d):
    picks = jnp.asarray((node_index()[d][:, None] == np.arange(5)[None, :]).astype(np.float32))
    return jnp.dot(jnp.dot(picks, matrix, precision=HIGH), picks.T, precision=HIGH)


def same_except(d):
    index = node_index()
    keep = np.ones((125, 125), bool)
    for other in range(3):
        if other != d:
            keep &= index[other][:, None] == index[other][None, :]
    return jnp.asarray(keep.astype(np.float32))


def operator_matrix(stiffness, flux):
    total = 0.0
    for d in range(3):
        sweep = spread(stiffness, d) * same_except(d)
        total = total + flux[d][:, None, :, None] * sweep[None, :, None, :]
    return total


def fine_matrix(local_factor, element_field_factor):
    local = spread(local_factor, 0) * spread(local_factor, 1) * spread(local_factor, 2)
    return element_field_factor[:, None, :, None] * local[None, :, None, :]


def face_halos(fine, dims):
    vecs, fields, elements = (fine.shape[0], fine.shape[1], fine.shape[3])
    cube = fine.reshape((vecs, fields, 5, 5, 5, elements))
    shaped = (vecs, fields, 25) + dims
    halos = []
    for d, name in enumerate(("gx", "gy", "gz")):
        minus = lax.index_in_dim(cube, 0, axis=2 + d, keepdims=False).reshape(shaped)
        plus = lax.index_in_dim(cube, 4, axis=2 + d, keepdims=False).reshape(shaped)
        after, before = neighbours(minus, plus, name, 3 + d)
        halos.append((minus, plus, after, before))
    return halos


def neighbour_ids(aggregate, dims):
    ids = aggregate.astype(jnp.float32).reshape(dims) + 1.0
    table = [ids]
    for d, name in enumerate(("gx", "gy", "gz")):
        after, before = neighbours(ids, ids, name, d)
        table += [after, before]
    return jnp.stack([t.reshape(-1) for t in table], 0)


def operate(field, halos, backs, dims, big, penalty):
    vecs, fields, elements = (field.shape[0], field.shape[1], field.shape[3])
    output = field + jnp.einsum("fqgp,kgpe->kfqe", big, field, precision=HIGH)
    result = output.reshape((vecs, fields, 5, 5, 5, elements))
    own = backs[0].reshape((vecs, fields, 1) + dims)
    for d in range(3):
        minus, plus, after, before = halos[d]
        after = after + backs[1 + 2 * d].reshape((vecs, fields, 1) + dims)
        before = before + backs[2 + 2 * d].reshape((vecs, fields, 1) + dims)
        tau = penalty[d][None, :, None, None, None, None]
        low = (tau * ((minus + own) - before)).reshape((vecs, fields, 5, 5, elements))
        high = (tau * ((plus + own) - after)).reshape((vecs, fields, 5, 5, elements))
        widths = [(0, 0)] * 6
        widths[2 + d] = (0, 4)
        result = result + jnp.pad(jnp.expand_dims(low, 2 + d), widths)
        widths[2 + d] = (4, 0)
        result = result + jnp.pad(jnp.expand_dims(high, 2 + d), widths)
    return result.reshape(field.shape)


def coarse_values(flat, onehot, picks, coarse_inverse):
    vecs, fields, elements = (flat.shape[0], flat.shape[1], flat.shape[3])
    nagg = coarse_inverse.shape[1] // fields
    means = jnp.sum(flat, axis=2) * (1.0 / 125.0)
    block = means.reshape(vecs * fields, elements)
    partial_sum = jnp.dot(block, onehot, precision=HIGH)
    restricted = group_sum(partial_sum, ("gz",), ("gy",))
    merged = restricted.reshape(vecs, fields * nagg)
    owned = jnp.einsum("kc,rc->kr", merged, coarse_inverse, precision=HIGH)
    coarse = group_gather(owned, ("gy", "gz"))
    values = jnp.dot(coarse.reshape(vecs * fields, nagg), picks, precision=HIGH)
    return values.reshape(vecs, fields, picks.shape[1] // elements, elements)


def on_device(
    vectors, stiffness, flux, penalty, local_factor, element_field_factor, aggregate, coarse_inverse
):
    big = operator_matrix(stiffness, flux)
    fine_op = fine_matrix(local_factor, element_field_factor)
    dims = tuple(vectors.shape[3:])
    elements = aggregate.size
    nagg = coarse_inverse.shape[1] // vectors.shape[1]
    onehot = (
        aggregate.reshape(elements)[:, None] == jnp.arange(nagg, dtype=jnp.int32)[None, :]
    ).astype(jnp.float32)
    ids = neighbour_ids(aggregate, dims).reshape(-1)
    labels = jnp.arange(1, nagg + 1, dtype=jnp.float32)
    picks = (labels[:, None] == ids[None, :]).astype(jnp.float32)
    flat = vectors.reshape(vectors.shape[:3] + (elements,))
    for turn in range(2):
        fine = jnp.einsum("fqgp,kgpe->kfqe", fine_op, flat, precision=HIGH)
        halos = face_halos(fine, dims)
        values = coarse_values(flat, onehot, picks, coarse_inverse)
        backs = [values[:, :, i] for i in range(values.shape[2])]
        own = backs[0].reshape(backs[0].shape[:2] + dims)
        after, before = neighbours(own, own, "gx", 2)
        backs[1], backs[2] = (after.reshape(backs[0].shape), before.reshape(backs[0].shape))
        flat = operate(fine + backs[0][:, :, None, :], halos, backs, dims, big, penalty)
    return flat.reshape(vectors.shape)


def solution(mesh):
    placed = (
        P(None, None, None, "gx", "gy", "gz"),
        P(),
        P(),
        P(),
        P(),
        P(),
        P("gx", "gy", "gz"),
        P(("gx", "gy", "gz"), None),
    )
    return jax.shard_map(
        on_device,
        mesh=mesh,
        in_specs=placed,
        out_specs=P(None, None, None, "gx", "gy", "gz"),
        check_vma=False,
    )
```

```python
import jax
import jax.numpy as jnp
import numpy as np
from jax import lax
from jax.sharding import PartitionSpec as P

HIGH = lax.Precision.HIGHEST


def neighbours(minus, plus, axis, dim):
    size, length = (lax.axis_size(axis), minus.shape[dim])
    up = [(i, i + 1) for i in range(size - 1)]
    down = [(i + 1, i) for i in range(size - 1)]
    last_plus = lax.slice_in_dim(plus, length - 1, length, axis=dim)
    first_minus = lax.slice_in_dim(minus, 0, 1, axis=dim)
    from_prev = lax.ppermute(last_plus, axis, up)
    from_next = lax.ppermute(first_minus, axis, down)
    before = jnp.concatenate([from_prev, lax.slice_in_dim(plus, 0, length - 1, axis=dim)], axis=dim)
    after = jnp.concatenate([lax.slice_in_dim(minus, 1, length, axis=dim), from_next], axis=dim)
    return after, before


def swap(x, axis, k):
    size = lax.axis_size(axis)
    return lax.ppermute(x, axis, [(i, i ^ k) for i in range(size)])


def bits_of(axes):
    order = []
    for axis in axes:
        size = lax.axis_size(axis)
        k = 1
        while k < size:
            order.append((axis, k))
            k *= 2
    return order


def is_pow2(n):
    return n > 0 and (n & (n - 1)) == 0


def group_sum(x, halved, exchanged):
    order = bits_of(halved)
    axes = tuple(halved) + tuple(exchanged)
    width = x.shape[-1]
    if not all(is_pow2(lax.axis_size(a)) for a in axes) or width % (1 << len(order)):
        return lax.psum(x, axes)
    for axis, k in order:
        bit = (lax.axis_index(axis) // k) % 2
        half = x.shape[-1] // 2
        low, high = x[..., :half], x[..., half:]
        send = jnp.where(bit == 0, high, low)
        keep = jnp.where(bit == 0, low, high)
        x = keep + swap(send, axis, k)
    for axis, k in bits_of(exchanged):
        x = x + swap(x, axis, k)
    for axis, k in reversed(order):
        bit = (lax.axis_index(axis) // k) % 2
        other = swap(x, axis, k)
        x = jnp.where(bit == 0, jnp.concatenate([x, other], -1), jnp.concatenate([other, x], -1))
    return x


def group_gather(y, axes):
    if not all(is_pow2(lax.axis_size(a)) for a in axes):
        return lax.all_gather(y, axes, axis=y.ndim - 1, tiled=True)
    width = y.shape[-1]
    order = [(axis, k) for axis in axes for (_, k) in bits_of((axis,))[::-1]]
    for axis, k in order:
        bit = (lax.axis_index(axis) // k) % 2
        other = swap(y, axis, k)
        y = jnp.where(bit == 0, jnp.concatenate([y, other], -1), jnp.concatenate([other, y], -1))
    lead = y.shape[:-1]
    count, nbits = (len(lead), len(order))
    y = y.reshape(lead + (2,) * nbits + (width,))
    perm = list(range(count)) + [count + nbits - 1 - i for i in range(nbits)] + [count + nbits]
    y = jnp.transpose(y, perm)
    return y.reshape(lead + (-1,))


def node_index():
    node = np.arange(125)
    return [node // 25, (node // 5) % 5, node % 5]


def spread(matrix, d):
    picks = jnp.asarray((node_index()[d][:, None] == np.arange(5)[None, :]).astype(np.float32))
    return jnp.dot(jnp.dot(picks, matrix, precision=HIGH), picks.T, precision=HIGH)


def same_except(d):
    index = node_index()
    keep = np.ones((125, 125), bool)
    for other in range(3):
        if other != d:
            keep &= index[other][:, None] == index[other][None, :]
    return jnp.asarray(keep.astype(np.float32))


def operator_matrix(stiffness, flux):
    total = 0.0
    for d in range(3):
        sweep = spread(stiffness, d) * same_except(d)
        total = total + flux[d][:, None, :, None] * sweep[None, :, None, :]
    return total


def fine_matrix(local_factor, element_field_factor):
    local = spread(local_factor, 0) * spread(local_factor, 1) * spread(local_factor, 2)
    return element_field_factor[:, None, :, None] * local[None, :, None, :]


def operate(flat, dims, big, penalty):
    vecs, fields, elements = (flat.shape[0], flat.shape[1], flat.shape[3])
    output = flat + jnp.einsum("fqgp,kgpe->kfqe", big, flat, precision=HIGH)
    cube = flat.reshape((vecs, fields, 5, 5, 5, elements))
    shaped = (vecs, fields, 25) + dims
    result = output.reshape(cube.shape)
    for d, name in enumerate(("gx", "gy", "gz")):
        minus = lax.index_in_dim(cube, 0, axis=2 + d, keepdims=False).reshape(shaped)
        plus = lax.index_in_dim(cube, 4, axis=2 + d, keepdims=False).reshape(shaped)
        after, before = neighbours(minus, plus, name, 3 + d)
        tau = penalty[d][None, :, None, None, None, None]
        low = (tau * (minus - before)).reshape((vecs, fields, 5, 5, elements))
        high = (tau * (plus - after)).reshape((vecs, fields, 5, 5, elements))
        widths = [(0, 0)] * 6
        widths[2 + d] = (0, 4)
        result = result + jnp.pad(jnp.expand_dims(low, 2 + d), widths)
        widths[2 + d] = (4, 0)
        result = result + jnp.pad(jnp.expand_dims(high, 2 + d), widths)
    return result.reshape(flat.shape)


def precondition(flat, fine_op, onehot, coarse_inverse):
    vecs, fields, elements = (flat.shape[0], flat.shape[1], flat.shape[3])
    fine = jnp.einsum("fqgp,kgpe->kfqe", fine_op, flat, precision=HIGH)
    nagg = coarse_inverse.shape[1] // fields
    means = jnp.sum(flat, axis=2) * (1.0 / 125.0)
    block = means.reshape(vecs * fields, elements)
    partial_sum = jnp.dot(block, onehot, precision=HIGH)
    restricted = group_sum(partial_sum, ("gz",), ("gy",))
    merged = restricted.reshape(vecs, fields * nagg)
    owned = jnp.einsum("kc,rc->kr", merged, coarse_inverse, precision=HIGH)
    coarse = group_gather(owned, ("gy", "gz"))
    values = jnp.dot(coarse.reshape(vecs * fields, nagg), onehot.T, precision=HIGH)
    back = values.reshape(vecs, fields, elements)
    return fine + back[:, :, None, :]


def on_device(
    vectors, stiffness, flux, penalty, local_factor, element_field_factor, aggregate, coarse_inverse
):
    big = operator_matrix(stiffness, flux)
    fine_op = fine_matrix(local_factor, element_field_factor)
    dims = tuple(vectors.shape[3:])
    elements = aggregate.size
    nagg = coarse_inverse.shape[1] // vectors.shape[1]
    onehot = (
        aggregate.reshape(elements)[:, None] == jnp.arange(nagg, dtype=jnp.int32)[None, :]
    ).astype(jnp.float32)
    flat = vectors.reshape(vectors.shape[:3] + (elements,))
    for turn in range(2):
        flat = precondition(flat, fine_op, onehot, coarse_inverse)
        flat = operate(flat, dims, big, penalty)
    return flat.reshape(vectors.shape)


def solution(mesh):
    placed = (
        P(None, None, None, "gx", "gy", "gz"),
        P(),
        P(),
        P(),
        P(),
        P(),
        P("gx", "gy", "gz"),
        P(("gx", "gy", "gz"), None),
    )
    return jax.shard_map(
        on_device,
        mesh=mesh,
        in_specs=placed,
        out_specs=P(None, None, None, "gx", "gy", "gz"),
        check_vma=False,
    )
```

```python
import jax
import jax.numpy as jnp
import numpy as np
from jax import lax
from jax.sharding import PartitionSpec as P

HIGH = lax.Precision.HIGHEST


def neighbours(minus, plus, axis, dim):
    size, length = (lax.axis_size(axis), minus.shape[dim])
    up = [(i, i + 1) for i in range(size - 1)]
    down = [(i + 1, i) for i in range(size - 1)]
    last_plus = lax.slice_in_dim(plus, length - 1, length, axis=dim)
    first_minus = lax.slice_in_dim(minus, 0, 1, axis=dim)
    from_prev = lax.ppermute(last_plus, axis, up)
    from_next = lax.ppermute(first_minus, axis, down)
    before = jnp.concatenate([from_prev, lax.slice_in_dim(plus, 0, length - 1, axis=dim)], axis=dim)
    after = jnp.concatenate([lax.slice_in_dim(minus, 1, length, axis=dim), from_next], axis=dim)
    return after, before


def swap(x, axis, k):
    size = lax.axis_size(axis)
    return lax.ppermute(x, axis, [(i, i ^ k) for i in range(size)])


def bits_of(axes):
    order = []
    for axis in axes:
        size = lax.axis_size(axis)
        k = 1
        while k < size:
            order.append((axis, k))
            k *= 2
    return order


def is_pow2(n):
    return n > 0 and (n & (n - 1)) == 0


def group_sum(x, halved, exchanged):
    axes = tuple(dict.fromkeys(a for a, _ in tuple(halved) + tuple(exchanged)))
    order = list(halved)
    width = x.shape[-1]
    if not all(is_pow2(lax.axis_size(a)) for a in axes) or width % (1 << len(order)):
        return lax.psum(x, axes)
    for axis, k in order:
        bit = (lax.axis_index(axis) // k) % 2
        half = x.shape[-1] // 2
        low, high = x[..., :half], x[..., half:]
        send = jnp.where(bit == 0, high, low)
        keep = jnp.where(bit == 0, low, high)
        x = keep + swap(send, axis, k)
    for axis, k in exchanged:
        x = x + swap(x, axis, k)
    for axis, k in reversed(order):
        bit = (lax.axis_index(axis) // k) % 2
        other = swap(x, axis, k)
        x = jnp.where(bit == 0, jnp.concatenate([x, other], -1), jnp.concatenate([other, x], -1))
    return x


def group_gather(y, axes):
    if not all(is_pow2(lax.axis_size(a)) for a in axes):
        return lax.all_gather(y, axes, axis=y.ndim - 1, tiled=True)
    width = y.shape[-1]
    for axis, k in bits_of(axes):
        bit = (lax.axis_index(axis) // k) % 2
        other = swap(y, axis, k)
        y = jnp.where(bit == 0, jnp.concatenate([y, other], -1), jnp.concatenate([other, y], -1))
    sizes = [lax.axis_size(a) for a in axes]
    lead = y.shape[:-1]
    y = y.reshape(lead + tuple(sizes[::-1]) + (width,))
    count = len(lead)
    perm = list(range(count)) + [count + len(axes) - 1 - i for i in range(len(axes))] + [count + len(axes)]
    y = jnp.transpose(y, perm)
    return y.reshape(lead + (-1,))


def node_index():
    node = np.arange(125)
    return [node // 25, (node // 5) % 5, node % 5]


def spread(matrix, d):
    picks = jnp.asarray((node_index()[d][:, None] == np.arange(5)[None, :]).astype(np.float32))
    return jnp.dot(jnp.dot(picks, matrix, precision=HIGH), picks.T, precision=HIGH)


def same_except(d):
    index = node_index()
    keep = np.ones((125, 125), bool)
    for other in range(3):
        if other != d:
            keep &= index[other][:, None] == index[other][None, :]
    return jnp.asarray(keep.astype(np.float32))


def operator_matrix(stiffness, flux):
    total = 0.0
    for d in range(3):
        sweep = spread(stiffness, d) * same_except(d)
        total = total + flux[d][:, None, :, None] * sweep[None, :, None, :]
    return total


def fine_matrix(local_factor, element_field_factor):
    local = spread(local_factor, 0) * spread(local_factor, 1) * spread(local_factor, 2)
    return element_field_factor[:, None, :, None] * local[None, :, None, :]


def operate(flat, dims, big, penalty):
    vecs, fields, elements = (flat.shape[0], flat.shape[1], flat.shape[3])
    output = flat + jnp.einsum("fqgp,kgpe->kfqe", big, flat, precision=HIGH)
    cube = flat.reshape((vecs, fields, 5, 5, 5, elements))
    shaped = (vecs, fields, 25) + dims
    result = output.reshape(cube.shape)
    for d, name in enumerate(("gx", "gy", "gz")):
        minus = lax.index_in_dim(cube, 0, axis=2 + d, keepdims=False).reshape(shaped)
        plus = lax.index_in_dim(cube, 4, axis=2 + d, keepdims=False).reshape(shaped)
        after, before = neighbours(minus, plus, name, 3 + d)
        tau = penalty[d][None, :, None, None, None, None]
        low = (tau * (minus - before)).reshape((vecs, fields, 5, 5, elements))
        high = (tau * (plus - after)).reshape((vecs, fields, 5, 5, elements))
        widths = [(0, 0)] * 6
        widths[2 + d] = (0, 4)
        result = result + jnp.pad(jnp.expand_dims(low, 2 + d), widths)
        widths[2 + d] = (4, 0)
        result = result + jnp.pad(jnp.expand_dims(high, 2 + d), widths)
    return result.reshape(flat.shape)


def precondition(flat, fine_op, onehot, coarse_inverse):
    vecs, fields, elements = (flat.shape[0], flat.shape[1], flat.shape[3])
    fine = jnp.einsum("fqgp,kgpe->kfqe", fine_op, flat, precision=HIGH)
    nagg = coarse_inverse.shape[1] // fields
    means = jnp.sum(flat, axis=2) * (1.0 / 125.0)
    block = means.reshape(vecs * fields, elements)
    partial_sum = jnp.dot(block, onehot, precision=HIGH)
    gz_bits, gy_bits = (bits_of(("gz",)), bits_of(("gy",)))
    restricted = group_sum(partial_sum, gz_bits[:2], gz_bits[2:] + gy_bits)
    merged = restricted.reshape(vecs, fields * nagg)
    owned = jnp.einsum("kc,rc->kr", merged, coarse_inverse, precision=HIGH)
    coarse = group_gather(owned, ("gy", "gz"))
    values = jnp.dot(coarse.reshape(vecs * fields, nagg), onehot.T, precision=HIGH)
    back = values.reshape(vecs, fields, elements)
    return fine + back[:, :, None, :]


def on_device(
    vectors, stiffness, flux, penalty, local_factor, element_field_factor, aggregate, coarse_inverse
):
    big = operator_matrix(stiffness, flux)
    fine_op = fine_matrix(local_factor, element_field_factor)
    dims = tuple(vectors.shape[3:])
    elements = aggregate.size
    nagg = coarse_inverse.shape[1] // vectors.shape[1]
    onehot = (
        aggregate.reshape(elements)[:, None] == jnp.arange(nagg, dtype=jnp.int32)[None, :]
    ).astype(jnp.float32)
    flat = vectors.reshape(vectors.shape[:3] + (elements,))
    for turn in range(2):
        flat = precondition(flat, fine_op, onehot, coarse_inverse)
        flat = operate(flat, dims, big, penalty)
    return flat.reshape(vectors.shape)


def solution(mesh):
    placed = (
        P(None, None, None, "gx", "gy", "gz"),
        P(),
        P(),
        P(),
        P(),
        P(),
        P("gx", "gy", "gz"),
        P(("gx", "gy", "gz"), None),
    )
    return jax.shard_map(
        on_device,
        mesh=mesh,
        in_specs=placed,
        out_specs=P(None, None, None, "gx", "gy", "gz"),
        check_vma=False,
    )
```

```python
import jax
import jax.numpy as jnp
import numpy as np
from jax import lax
from jax.sharding import PartitionSpec as P

HIGH = lax.Precision.HIGHEST


def neighbours(minus, plus, axis, dim):
    size, length = (lax.axis_size(axis), minus.shape[dim])
    up = [(i, i + 1) for i in range(size - 1)]
    down = [(i + 1, i) for i in range(size - 1)]
    last_plus = lax.slice_in_dim(plus, length - 1, length, axis=dim)
    first_minus = lax.slice_in_dim(minus, 0, 1, axis=dim)
    from_prev = lax.ppermute(last_plus, axis, up)
    from_next = lax.ppermute(first_minus, axis, down)
    before = jnp.concatenate([from_prev, lax.slice_in_dim(plus, 0, length - 1, axis=dim)], axis=dim)
    after = jnp.concatenate([lax.slice_in_dim(minus, 1, length, axis=dim), from_next], axis=dim)
    return after, before


def swap(x, axis, k):
    size = lax.axis_size(axis)
    return lax.ppermute(x, axis, [(i, i ^ k) for i in range(size)])


def bits_of(axes):
    order = []
    for axis in axes:
        size = lax.axis_size(axis)
        k = 1
        while k < size:
            order.append((axis, k))
            k *= 2
    return order


def is_pow2(n):
    return n > 0 and (n & (n - 1)) == 0


def group_sum(x, halved, exchanged):
    axes = tuple(dict.fromkeys(a for a, _ in tuple(halved) + tuple(exchanged)))
    order = list(halved)
    width = x.shape[-1]
    if not all(is_pow2(lax.axis_size(a)) for a in axes) or width % (1 << len(order)):
        return lax.psum(x, axes)
    for axis, k in order:
        bit = (lax.axis_index(axis) // k) % 2
        half = x.shape[-1] // 2
        low, high = x[..., :half], x[..., half:]
        send = jnp.where(bit == 0, high, low)
        keep = jnp.where(bit == 0, low, high)
        x = keep + swap(send, axis, k)
    for axis, k in exchanged:
        x = x + swap(x, axis, k)
    for axis, k in reversed(order):
        bit = (lax.axis_index(axis) // k) % 2
        other = swap(x, axis, k)
        x = jnp.where(bit == 0, jnp.concatenate([x, other], -1), jnp.concatenate([other, x], -1))
    return x


def group_gather(y, axes):
    if not all(is_pow2(lax.axis_size(a)) for a in axes):
        return lax.all_gather(y, axes, axis=y.ndim - 1, tiled=True)
    width = y.shape[-1]
    for axis, k in bits_of(axes):
        bit = (lax.axis_index(axis) // k) % 2
        other = swap(y, axis, k)
        y = jnp.where(bit == 0, jnp.concatenate([y, other], -1), jnp.concatenate([other, y], -1))
    sizes = [lax.axis_size(a) for a in axes]
    lead = y.shape[:-1]
    y = y.reshape(lead + tuple(sizes[::-1]) + (width,))
    count = len(lead)
    perm = list(range(count)) + [count + len(axes) - 1 - i for i in range(len(axes))] + [count + len(axes)]
    y = jnp.transpose(y, perm)
    return y.reshape(lead + (-1,))


def node_index():
    node = np.arange(125)
    return [node // 25, (node // 5) % 5, node % 5]


def spread(matrix, d):
    picks = jnp.asarray((node_index()[d][:, None] == np.arange(5)[None, :]).astype(np.float32))
    return jnp.dot(jnp.dot(picks, matrix, precision=HIGH), picks.T, precision=HIGH)


def same_except(d):
    index = node_index()
    keep = np.ones((125, 125), bool)
    for other in range(3):
        if other != d:
            keep &= index[other][:, None] == index[other][None, :]
    return jnp.asarray(keep.astype(np.float32))


def operator_matrix(stiffness, flux):
    total = 0.0
    for d in range(3):
        sweep = spread(stiffness, d) * same_except(d)
        total = total + flux[d][:, None, :, None] * sweep[None, :, None, :]
    return total


def fine_matrix(local_factor, element_field_factor):
    local = spread(local_factor, 0) * spread(local_factor, 1) * spread(local_factor, 2)
    return element_field_factor[:, None, :, None] * local[None, :, None, :]


def operate(flat, dims, big, penalty):
    vecs, fields, elements = (flat.shape[0], flat.shape[1], flat.shape[3])
    output = flat + jnp.einsum("fqgp,kgpe->kfqe", big, flat, precision=HIGH)
    cube = flat.reshape((vecs, fields, 5, 5, 5, elements))
    shaped = (vecs, fields, 25) + dims
    result = output.reshape(cube.shape)
    for d, name in enumerate(("gx", "gy", "gz")):
        minus = lax.index_in_dim(cube, 0, axis=2 + d, keepdims=False).reshape(shaped)
        plus = lax.index_in_dim(cube, 4, axis=2 + d, keepdims=False).reshape(shaped)
        after, before = neighbours(minus, plus, name, 3 + d)
        tau = penalty[d][None, :, None, None, None, None]
        low = (tau * (minus - before)).reshape((vecs, fields, 5, 5, elements))
        high = (tau * (plus - after)).reshape((vecs, fields, 5, 5, elements))
        widths = [(0, 0)] * 6
        widths[2 + d] = (0, 4)
        result = result + jnp.pad(jnp.expand_dims(low, 2 + d), widths)
        widths[2 + d] = (4, 0)
        result = result + jnp.pad(jnp.expand_dims(high, 2 + d), widths)
    return result.reshape(flat.shape)


def precondition(flat, fine_op, onehot, coarse_inverse):
    vecs, fields, elements = (flat.shape[0], flat.shape[1], flat.shape[3])
    fine = jnp.einsum("fqgp,kgpe->kfqe", fine_op, flat, precision=HIGH)
    nagg = coarse_inverse.shape[1] // fields
    means = jnp.sum(flat, axis=2) * (1.0 / 125.0)
    block = means.reshape(vecs * fields, elements)
    partial_sum = jnp.dot(block, onehot, precision=HIGH)
    gz_bits, gy_bits = (bits_of(("gz",)), bits_of(("gy",)))
    restricted = group_sum(partial_sum, gz_bits[:1], gz_bits[1:] + gy_bits)
    merged = restricted.reshape(vecs, fields * nagg)
    owned = jnp.einsum("kc,rc->kr", merged, coarse_inverse, precision=HIGH)
    coarse = group_gather(owned, ("gy", "gz"))
    values = jnp.dot(coarse.reshape(vecs * fields, nagg), onehot.T, precision=HIGH)
    back = values.reshape(vecs, fields, elements)
    return fine + back[:, :, None, :]


def on_device(
    vectors, stiffness, flux, penalty, local_factor, element_field_factor, aggregate, coarse_inverse
):
    big = operator_matrix(stiffness, flux)
    fine_op = fine_matrix(local_factor, element_field_factor)
    dims = tuple(vectors.shape[3:])
    elements = aggregate.size
    nagg = coarse_inverse.shape[1] // vectors.shape[1]
    onehot = (
        aggregate.reshape(elements)[:, None] == jnp.arange(nagg, dtype=jnp.int32)[None, :]
    ).astype(jnp.float32)
    flat = vectors.reshape(vectors.shape[:3] + (elements,))
    for turn in range(2):
        flat = precondition(flat, fine_op, onehot, coarse_inverse)
        flat = operate(flat, dims, big, penalty)
    return flat.reshape(vectors.shape)


def solution(mesh):
    placed = (
        P(None, None, None, "gx", "gy", "gz"),
        P(),
        P(),
        P(),
        P(),
        P(),
        P("gx", "gy", "gz"),
        P(("gx", "gy", "gz"), None),
    )
    return jax.shard_map(
        on_device,
        mesh=mesh,
        in_specs=placed,
        out_specs=P(None, None, None, "gx", "gy", "gz"),
        check_vma=False,
    )
```
